32 devices in a mesh: tx: 16 (over z, y, x), ty: 2 (over core).
Axes of the slice: x: 2, y: 2, z: 4, core: 2. Of those that a mesh axis runs over, the one named last changes fastest.
Arguments:
- pulses: bfloat16 [32, 2, 16384], P(('tx', 'ty')), may hold values from -6 to 6
- geometry: bfloat16 [5, 32], P(None, ('tx', 'ty')), as said below
- footprint: int32 [32, 8], P(('tx', 'ty')), may hold values from 0 to 15, as said below
- offsets: int32 [32, 16], P(None, 'tx'), may hold values from 0 to 15352
- image_in: float32 [2, 8192, 1024], P(None, 'tx', 'ty'), may hold values from -6 to 6
Outputs:
- image_out: float32 [2, 8192, 1024], P(None, 'tx', 'ty')
The draws below stay inside these ranges and needn't reach their ends.
Inputs may be any that keep to these rules, and one draw needn't show every extreme that they name: `footprint`: each row is a run of 8 consecutive tile-row indices in ascending order. `geometry`: row 0 lies in 0.002 to 0.05, rows 1 and 4 in -pi to pi, row 2 in -0.05 to 0.05, row 3 in -0.02 to 0.02.
All inputs are finite; a program needn't handle non-finite values.
Results may differ from the reference program's by a relative error of at most 0.0027.
Values may be sent and summed in bfloat16 or wider, within the bound.
No kernel may reach another device: no remote copies, remote signals or barrier semaphores. Data moves between devices by JAX's collectives and lax.ppermute only.
A program may use at most 64 MiB of HBM per device.

```python
import math
import jax
import jax.numpy as jnp
from jax import lax

NS = 16384
TAPS = 8
ROWS_T = 512
PULSES = 32
FOOT = 8
ROWS = 8192
COLS = 1024
N_TX = 16


def draw_geometry(key, part):
    keys = jax.random.split(key, 5)
    rate = jax.random.uniform(keys[0], (PULSES,), jnp.float32, 0.002, 0.05)
    shift = jax.random.uniform(keys[1], (PULSES,), jnp.float32, -math.pi, math.pi)
    ramp = jax.random.uniform(keys[2], (PULSES,), jnp.float32, -0.05, 0.05)
    tilt = jax.random.uniform(keys[3], (PULSES,), jnp.float32, -0.02, 0.02)
    base_phase = jax.random.uniform(keys[4], (PULSES,), jnp.float32, -math.pi, math.pi)
    return jnp.stack([rate, shift, ramp, tilt, base_phase]).astype(jnp.bfloat16)


def draw_footprint(key, part):
    keys = jax.random.split(key, 3)
    starts = jax.random.randint(keys[0], (PULSES,), 0, N_TX - FOOT + 1).astype(jnp.int32)
    first = jax.random.randint(keys[1], (), 0, PULSES).astype(jnp.int32)
    step = jax.random.randint(keys[2], (), 1, PULSES).astype(jnp.int32)
    second = (first + step) % PULSES
    places = jnp.arange(PULSES, dtype=jnp.int32)
    starts = jnp.where(places == first, jnp.zeros((), jnp.int32), starts)
    starts = jnp.where(places == second, jnp.full((), N_TX - FOOT, jnp.int32), starts)
    return (starts[:, None] + jnp.arange(FOOT, dtype=jnp.int32)[None, :]).astype(jnp.int32)


def touch_ends(values, own_key, least, high):
    index_at = [jax.random.randint(jax.random.fold_in(own_key, axis), (), 0, length) for axis, length in enumerate(values.shape)]
    longest = values.shape.index(max(values.shape))
    neighbour = index_at[:longest] + [(index_at[longest] + 1) % values.shape[longest]] + index_at[longest + 1:]
    return values.at[tuple(index_at)].set(least).at[tuple(neighbour)].set(high)


def block_scale(own_key, dims, pieces, smallest, high):
    loudness = 1.0
    for dim, blocks in pieces:
        steps = jax.random.uniform(jax.random.fold_in(jax.random.fold_in(own_key, 6), dim), (blocks,), jnp.float32, smallest / len(pieces), high / len(pieces))
        loudness = loudness * jnp.repeat(jnp.exp(steps), dims[dim] // blocks).reshape((-1,) + (1,) * (len(dims) - 1 - dim))
    return loudness


def centred(stream_key, extent, deviation, most, cuts=(), held_as=jnp.bfloat16):
    drawn = deviation * jax.random.normal(stream_key, extent, jnp.float32)
    if cuts:
        drawn = drawn * block_scale(stream_key, extent, cuts, -0.22, 0.18)
    return jnp.clip(drawn, -most, most).astype(held_as)


def setup_inputs(seed: int = 0) -> dict:
    key_list = jax.random.split(jax.random.key(seed), 6)
    return {
        "pulses": centred(key_list[0], (PULSES, 2, NS), 1.0, 6.0, ((0, 32),)),
        "geometry": draw_geometry(jax.random.fold_in(key_list[5], 71), 0),
        "footprint": draw_footprint(jax.random.fold_in(key_list[5], 71), 0),
        "offsets": touch_ends(jax.random.randint(key_list[3], (PULSES, N_TX), 0, NS - COLS - TAPS + 1), jax.random.fold_in(key_list[3], 1), 0, NS - COLS - TAPS).astype(jnp.int32),
        "image_in": centred(key_list[4], (2, ROWS, COLS), 1.0, 6.0, ((1, 16), (2, 2)), jnp.float32),
    }


def make_taps(geometry, columns):
    rate = geometry[0].astype(jnp.float32)[:, None]
    shift = geometry[1].astype(jnp.float32)[:, None]
    ramp = geometry[2].astype(jnp.float32)[:, None]
    fraction = 0.5 + 0.45 * jnp.sin(rate * columns[None, :] + shift)
    places = jnp.arange(TAPS).astype(jnp.float32)
    spread = places[None, :, None] - 3.0 - fraction[:, None, :]
    angle_x = jnp.pi * spread
    kernel = jnp.sin(angle_x) / angle_x * (0.54 + 0.46 * jnp.cos(angle_x / 4.0))
    turning = ramp * columns[None, :]
    real_part = kernel * jnp.cos(turning)[:, None, :]
    imag_part = kernel * jnp.sin(turning)[:, None, :]
    return jnp.concatenate([real_part, imag_part], axis=1).astype(jnp.bfloat16)

def interpolate(windows, taps, width):
    real_sum = jnp.zeros((windows.shape[0], width), jnp.float32)
    imag_sum = jnp.zeros((windows.shape[0], width), jnp.float32)
    for k in range(TAPS):
        segment = windows[:, :, k:k + width].astype(jnp.float32)
        tap_real = taps[:, k].astype(jnp.float32)
        tap_imag = taps[:, TAPS + k].astype(jnp.float32)
        real_sum = real_sum + tap_real * segment[:, 0] - tap_imag * segment[:, 1]
        imag_sum = imag_sum + tap_real * segment[:, 1] + tap_imag * segment[:, 0]
    return jnp.concatenate([real_sum, imag_sum], axis=0).astype(jnp.bfloat16)

def phase_matrix(tilt, base_phase, rows):
    angles = rows[:, None] * tilt.astype(jnp.float32)[None, :] + base_phase.astype(jnp.float32)[None, :]
    cosine = jnp.cos(angles).astype(jnp.bfloat16)
    sine = jnp.sin(angles).astype(jnp.bfloat16)
    upper = jnp.concatenate([cosine, -sine], axis=1)
    lower = jnp.concatenate([sine, cosine], axis=1)
    return jnp.concatenate([upper, lower], axis=0)

def cut_window(signal, start):
    return lax.dynamic_slice_in_dim(signal, start, COLS + TAPS, 1)

def reference(pulses, geometry, footprint, offsets, image_in):
    live = jnp.any(footprint[:, :, None] == jnp.arange(N_TX, dtype=jnp.int32)[None, None, :], axis=1)
    taps = make_taps(geometry, jnp.arange(COLS).astype(jnp.float32))

    def tile_row(index):
        starts = lax.dynamic_index_in_dim(offsets, index, 1, keepdims=False)
        windows = jax.vmap(cut_window)(pulses, starts)
        values = interpolate(windows, taps, COLS)
        live_here = lax.dynamic_index_in_dim(live, index, 1, keepdims=False)
        doubled = jnp.concatenate([live_here, live_here])
        values = jnp.where(doubled[:, None], values, jnp.zeros((), jnp.bfloat16))
        rows = (index * ROWS_T + jnp.arange(ROWS_T, dtype=jnp.int32)).astype(jnp.float32)
        left = phase_matrix(geometry[3], geometry[4], rows)
        return jnp.dot(left, values, preferred_element_type=jnp.float32).reshape(2, ROWS_T, COLS)
    blocks = lax.map(tile_row, jnp.arange(N_TX, dtype=jnp.int32))
    blocks = jnp.transpose(blocks, (1, 0, 2, 3)).reshape(2, ROWS, COLS)
    scale = 1.0 / math.sqrt(PULSES)
    return image_in + scale * blocks
```

```python
import math

import jax
import jax.numpy as jnp
from jax import lax
from jax.sharding import PartitionSpec as P

TAPS = 8


def make_taps(geometry, columns):
    rate = geometry[0].astype(jnp.float32)[:, None]
    shift = geometry[1].astype(jnp.float32)[:, None]
    ramp = geometry[2].astype(jnp.float32)[:, None]
    fraction = 0.5 + 0.45 * jnp.sin(rate * columns[None, :] + shift)
    places = jnp.arange(TAPS).astype(jnp.float32)
    spread = places[None, :, None] - 3.0 - fraction[:, None, :]
    angle_x = jnp.pi * spread
    kernel = jnp.sin(angle_x) / angle_x * (0.54 + 0.46 * jnp.cos(angle_x / 4.0))
    turning = ramp * columns[None, :]
    real_part = kernel * jnp.cos(turning)[:, None, :]
    imag_part = kernel * jnp.sin(turning)[:, None, :]
    return jnp.concatenate([real_part, imag_part], axis=1).astype(jnp.bfloat16)


def interpolate(windows, taps, width):
    real_sum = jnp.zeros((windows.shape[0], width), jnp.float32)
    imag_sum = jnp.zeros((windows.shape[0], width), jnp.float32)
    for k in range(TAPS):
        segment = windows[:, :, k : k + width].astype(jnp.float32)
        tap_real = taps[:, k].astype(jnp.float32)
        tap_imag = taps[:, TAPS + k].astype(jnp.float32)
        real_sum = real_sum + tap_real * segment[:, 0] - tap_imag * segment[:, 1]
        imag_sum = imag_sum + tap_real * segment[:, 1] + tap_imag * segment[:, 0]
    return jnp.concatenate([real_sum, imag_sum], axis=0).astype(jnp.bfloat16)


def phase_matrix(tilt, base_phase, rows):
    angles = (
        rows[:, None] * tilt.astype(jnp.float32)[None, :] + base_phase.astype(jnp.float32)[None, :]
    )
    cosine = jnp.cos(angles).astype(jnp.bfloat16)
    sine = jnp.sin(angles).astype(jnp.bfloat16)
    upper = jnp.concatenate([cosine, -sine], axis=1)
    lower = jnp.concatenate([sine, cosine], axis=1)
    return jnp.concatenate([upper, lower], axis=0)


def body(pulses, geometry, footprint, offsets, image_in):
    count_rows = lax.axis_size("tx")
    count_cols = lax.axis_size("ty")
    devices_all = count_rows * count_cols
    held = pulses.shape[0]
    slots = devices_all * held
    tiles_here = offsets.shape[1]
    tiles_all = count_rows * tiles_here
    rows_here = image_in.shape[1]
    tile_rows_n = rows_here // tiles_here
    tile_cols_n = image_in.shape[2]
    length = tile_cols_n + TAPS
    row_index = lax.axis_index("tx")
    col_index = lax.axis_index("ty")

    geo_send = jnp.broadcast_to(geometry.T[None], (devices_all, held, 5))
    got_geo = lax.all_to_all(geo_send, ("tx", "ty"), 0, 0, tiled=True)

    by_holder = offsets.reshape(count_rows, count_cols, held, tiles_here)
    off_send = lax.dynamic_index_in_dim(by_holder, col_index, 1, keepdims=False)
    off_got = lax.all_to_all(off_send, "tx", 0, 0, tiled=True)
    mine = jnp.transpose(off_got, (1, 0, 2)).reshape(held, tiles_all)

    live = jnp.any(
        footprint[:, :, None] == jnp.arange(tiles_all, dtype=jnp.int32)[None, None, :], axis=1
    )

    pieces = []
    for a in range(count_rows):
        for b in range(count_cols):
            for h in range(held):
                for r in range(tiles_here):
                    t = a * tiles_here + r
                    start = mine[h, t] + b * tile_cols_n
                    cut = lax.dynamic_slice_in_dim(pulses[h], start, length, 1)
                    pieces.append(jnp.where(live[h, t], cut, jnp.zeros((), cut.dtype)))
    windows = jnp.stack(pieces).reshape(devices_all, held * tiles_here, 2, length)
    got_windows = lax.all_to_all(windows, ("tx", "ty"), 0, 0, tiled=True)
    got_windows = got_windows.reshape(slots, tiles_here, 2, length)

    got_geo = got_geo.reshape(slots, 5).T
    columns = (col_index * tile_cols_n + jnp.arange(tile_cols_n, dtype=jnp.int32)).astype(
        jnp.float32
    )
    got_taps = make_taps(got_geo, columns)
    scale = 1.0 / math.sqrt(slots)
    outs = []
    for r in range(tiles_here):
        values = interpolate(got_windows[:, r], got_taps, tile_cols_n)
        rows = (
            row_index * rows_here + r * tile_rows_n + jnp.arange(tile_rows_n, dtype=jnp.int32)
        ).astype(jnp.float32)
        left = phase_matrix(got_geo[3], got_geo[4], rows)
        product = jnp.dot(left, values, preferred_element_type=jnp.float32).reshape(
            2, tile_rows_n, tile_cols_n
        )
        outs.append(product)
    product = outs[0] if tiles_here == 1 else jnp.concatenate(outs, axis=1)
    return image_in + scale * product


def solution(mesh):
    in_specs = (
        P(("tx", "ty"), None, None),
        P(None, ("tx", "ty")),
        P(("tx", "ty"), None),
        P(None, "tx"),
        P(None, "tx", "ty"),
    )
    out_specs = P(None, "tx", "ty")
    return jax.shard_map(body, mesh=mesh, in_specs=in_specs, out_specs=out_specs, check_vma=False)
```

```python
import math

import jax
import jax.numpy as jnp
from jax import lax
from jax.sharding import PartitionSpec as P

TAPS = 8


def make_taps(geometry, columns):
    rate = geometry[0].astype(jnp.float32)[:, None]
    shift = geometry[1].astype(jnp.float32)[:, None]
    ramp = geometry[2].astype(jnp.float32)[:, None]
    fraction = 0.5 + 0.45 * jnp.sin(rate * columns[None, :] + shift)
    places = jnp.arange(TAPS).astype(jnp.float32)
    spread = places[None, :, None] - 3.0 - fraction[:, None, :]
    angle_x = jnp.pi * spread
    kernel = jnp.sin(angle_x) / angle_x * (0.54 + 0.46 * jnp.cos(angle_x / 4.0))
    turning = ramp * columns[None, :]
    real_part = kernel * jnp.cos(turning)[:, None, :]
    imag_part = kernel * jnp.sin(turning)[:, None, :]
    return jnp.concatenate([real_part, imag_part], axis=1).astype(jnp.bfloat16)


def interpolate(windows, taps, width):
    real_sum = jnp.zeros((windows.shape[0], width), jnp.float32)
    imag_sum = jnp.zeros((windows.shape[0], width), jnp.float32)
    for k in range(TAPS):
        segment = windows[:, :, k : k + width].astype(jnp.float32)
        tap_real = taps[:, k].astype(jnp.float32)
        tap_imag = taps[:, TAPS + k].astype(jnp.float32)
        real_sum = real_sum + tap_real * segment[:, 0] - tap_imag * segment[:, 1]
        imag_sum = imag_sum + tap_real * segment[:, 1] + tap_imag * segment[:, 0]
    return jnp.concatenate([real_sum, imag_sum], axis=0).astype(jnp.bfloat16)


def phase_matrix(tilt, base_phase, rows):
    angles = (
        rows[:, None] * tilt.astype(jnp.float32)[None, :] + base_phase.astype(jnp.float32)[None, :]
    )
    cosine = jnp.cos(angles).astype(jnp.bfloat16)
    sine = jnp.sin(angles).astype(jnp.bfloat16)
    upper = jnp.concatenate([cosine, -sine], axis=1)
    lower = jnp.concatenate([sine, cosine], axis=1)
    return jnp.concatenate([upper, lower], axis=0)


def body(pulses, geometry, footprint, offsets, image_in):
    count_rows = lax.axis_size("tx")
    count_cols = lax.axis_size("ty")
    devices_all = count_rows * count_cols
    held = pulses.shape[0]
    slots = devices_all * held
    tiles_here = offsets.shape[1]
    tiles_all = count_rows * tiles_here
    rows_here = image_in.shape[1]
    tile_rows_n = rows_here // tiles_here
    tile_cols_n = image_in.shape[2]
    length = tile_cols_n + TAPS
    row_index = lax.axis_index("tx")
    col_index = lax.axis_index("ty")

    geo_send = jnp.broadcast_to(geometry.T[None], (devices_all, held, 5))
    got_geo = lax.all_to_all(geo_send, ("tx", "ty"), 0, 0, tiled=True)

    by_holder = offsets.reshape(count_rows, count_cols, held, tiles_here)
    off_send = lax.dynamic_index_in_dim(by_holder, col_index, 1, keepdims=False)
    off_got = lax.all_to_all(off_send, "tx", 0, 0, tiled=True)
    mine = jnp.transpose(off_got, (1, 0, 2)).reshape(held, tiles_all)

    live = jnp.any(
        footprint[:, :, None] == jnp.arange(tiles_all, dtype=jnp.int32)[None, None, :], axis=1
    )

    lanes = 128
    row_count = pulses.shape[2] // lanes
    span = 6
    signal = pulses.reshape(held, 2, row_count, lanes)
    starts = jnp.transpose(mine.reshape(held, count_rows, 1, tiles_here), (0, 1, 2, 3))
    starts = starts + (jnp.arange(count_cols, dtype=jnp.int32) * tile_cols_n)[None, None, :, None]
    starts = starts.reshape(held, -1)
    lit = jnp.broadcast_to(
        jnp.transpose(live.reshape(held, count_rows, 1, tiles_here), (0, 1, 2, 3)),
        (held, count_rows, count_cols, tiles_here),
    ).reshape(held, -1)
    first_row = starts // lanes
    shift = starts % lanes
    row_pick = (
        jnp.arange(row_count, dtype=jnp.int32)[None, None, None, :]
        == first_row[:, :, None, None] + jnp.arange(span, dtype=jnp.int32)[None, None, :, None]
    ) & lit[:, :, None, None]
    gathered = jnp.einsum(
        "hwjn,hcnl->hwcjl",
        row_pick.astype(pulses.dtype),
        signal,
        preferred_element_type=jnp.float32,
    ).astype(pulses.dtype)
    paired = jnp.concatenate([gathered[:, :, :, :-1], gathered[:, :, :, 1:]], axis=-1)
    lane_pick = (
        jnp.arange(2 * lanes, dtype=jnp.int32)[None, None, :, None]
        == shift[:, :, None, None] + jnp.arange(lanes, dtype=jnp.int32)[None, None, None, :]
    )
    shifted = jnp.einsum(
        "hwcjm,hwml->hwcjl",
        paired,
        lane_pick.astype(pulses.dtype),
        preferred_element_type=jnp.float32,
    ).astype(pulses.dtype)
    shifted = shifted.reshape(held, count_rows, count_cols, tiles_here, 2, (span - 1) * lanes)
    shifted = shifted[..., :length]
    windows = jnp.transpose(shifted, (1, 2, 0, 3, 4, 5)).reshape(
        devices_all, held * tiles_here, 2, length
    )
    got_windows = lax.all_to_all(windows, ("tx", "ty"), 0, 0, tiled=True)
    got_windows = got_windows.reshape(slots, tiles_here, 2, length)

    got_geo = got_geo.reshape(slots, 5).T
    columns = (col_index * tile_cols_n + jnp.arange(tile_cols_n, dtype=jnp.int32)).astype(
        jnp.float32
    )
    got_taps = make_taps(got_geo, columns)
    scale = 1.0 / math.sqrt(slots)
    outs = []
    for r in range(tiles_here):
        values = interpolate(got_windows[:, r], got_taps, tile_cols_n)
        rows = (
            row_index * rows_here + r * tile_rows_n + jnp.arange(tile_rows_n, dtype=jnp.int32)
        ).astype(jnp.float32)
        left = phase_matrix(got_geo[3], got_geo[4], rows)
        product = jnp.dot(left, values, preferred_element_type=jnp.float32).reshape(
            2, tile_rows_n, tile_cols_n
        )
        outs.append(product)
    product = outs[0] if tiles_here == 1 else jnp.concatenate(outs, axis=1)
    return image_in + scale * product


def solution(mesh):
    in_specs = (
        P(("tx", "ty"), None, None),
        P(None, ("tx", "ty")),
        P(("tx", "ty"), None),
        P(None, "tx"),
        P(None, "tx", "ty"),
    )
    out_specs = P(None, "tx", "ty")
    return jax.shard_map(body, mesh=mesh, in_specs=in_specs, out_specs=out_specs, check_vma=False)
```

```python
import math

import jax
import jax.numpy as jnp
from jax import lax
from jax.sharding import PartitionSpec as P

TAPS = 8


def make_taps(geometry, columns):
    rate = geometry[0].astype(jnp.float32)[:, None]
    shift = geometry[1].astype(jnp.float32)[:, None]
    ramp = geometry[2].astype(jnp.float32)[:, None]
    fraction = 0.5 + 0.45 * jnp.sin(rate * columns[None, :] + shift)
    places = jnp.arange(TAPS).astype(jnp.float32)
    spread = places[None, :, None] - 3.0 - fraction[:, None, :]
    angle_x = jnp.pi * spread
    kernel = jnp.sin(angle_x) / angle_x * (0.54 + 0.46 * jnp.cos(angle_x / 4.0))
    turning = ramp * columns[None, :]
    real_part = kernel * jnp.cos(turning)[:, None, :]
    imag_part = kernel * jnp.sin(turning)[:, None, :]
    return jnp.concatenate([real_part, imag_part], axis=1).astype(jnp.bfloat16)


def interpolate(windows, taps, width):
    real_sum = jnp.zeros((windows.shape[0], width), jnp.float32)
    imag_sum = jnp.zeros((windows.shape[0], width), jnp.float32)
    for k in range(TAPS):
        segment = windows[:, :, k : k + width].astype(jnp.float32)
        tap_real = taps[:, k].astype(jnp.float32)
        tap_imag = taps[:, TAPS + k].astype(jnp.float32)
        real_sum = real_sum + tap_real * segment[:, 0] - tap_imag * segment[:, 1]
        imag_sum = imag_sum + tap_real * segment[:, 1] + tap_imag * segment[:, 0]
    return jnp.concatenate([real_sum, imag_sum], axis=0).astype(jnp.bfloat16)


def phase_matrix(tilt, base_phase, rows):
    angles = (
        rows[:, None] * tilt.astype(jnp.float32)[None, :] + base_phase.astype(jnp.float32)[None, :]
    )
    cosine = jnp.cos(angles).astype(jnp.bfloat16)
    sine = jnp.sin(angles).astype(jnp.bfloat16)
    upper = jnp.concatenate([cosine, -sine], axis=1)
    lower = jnp.concatenate([sine, cosine], axis=1)
    return jnp.concatenate([upper, lower], axis=0)


def body(pulses, geometry, footprint, offsets, image_in):
    count_rows = lax.axis_size("tx")
    count_cols = lax.axis_size("ty")
    devices_all = count_rows * count_cols
    held = pulses.shape[0]
    slots = devices_all * held
    tiles_here = offsets.shape[1]
    tiles_all = count_rows * tiles_here
    rows_here = image_in.shape[1]
    tile_rows_n = rows_here // tiles_here
    tile_cols_n = image_in.shape[2]
    length = tile_cols_n + TAPS
    row_index = lax.axis_index("tx")
    col_index = lax.axis_index("ty")

    by_holder = offsets.reshape(count_rows, count_cols, held, tiles_here)
    off_send = lax.dynamic_index_in_dim(by_holder, col_index, 1, keepdims=False)
    off_got = lax.all_to_all(off_send, "tx", 0, 0, tiled=True)
    mine = jnp.transpose(off_got, (1, 0, 2)).reshape(held, tiles_all)

    live = jnp.any(
        footprint[:, :, None] == jnp.arange(tiles_all, dtype=jnp.int32)[None, None, :], axis=1
    )

    lanes = 128
    row_count = pulses.shape[2] // lanes
    span = 6
    signal = pulses.reshape(held, 2, row_count, lanes)
    starts = mine.reshape(held, count_rows, 1, tiles_here)
    starts = starts + (jnp.arange(count_cols, dtype=jnp.int32) * tile_cols_n)[None, None, :, None]
    starts = starts.reshape(held, -1)
    lit = jnp.broadcast_to(
        live.reshape(held, count_rows, 1, tiles_here), (held, count_rows, count_cols, tiles_here)
    ).reshape(held, -1)
    first_row = starts // lanes
    shift = starts % lanes
    row_pick = (
        jnp.arange(row_count, dtype=jnp.int32)[None, None, None, :]
        == first_row[:, :, None, None] + jnp.arange(span, dtype=jnp.int32)[None, None, :, None]
    ) & lit[:, :, None, None]
    gathered = jnp.einsum(
        "hwjn,hcnl->hwcjl",
        row_pick.astype(pulses.dtype),
        signal,
        preferred_element_type=jnp.float32,
    ).astype(pulses.dtype)
    paired = jnp.concatenate([gathered[:, :, :, :-1], gathered[:, :, :, 1:]], axis=-1)
    lane_pick = (
        jnp.arange(2 * lanes, dtype=jnp.int32)[None, None, :, None]
        == shift[:, :, None, None] + jnp.arange(lanes, dtype=jnp.int32)[None, None, None, :]
    )
    shifted = jnp.einsum(
        "hwcjm,hwml->hwcjl",
        paired,
        lane_pick.astype(pulses.dtype),
        preferred_element_type=jnp.float32,
    ).astype(pulses.dtype)
    shifted = shifted.reshape(held, count_rows, count_cols, tiles_here, 2, (span - 1) * lanes)
    shifted = shifted[..., :length]

    columns = (
        jnp.arange(count_cols, dtype=jnp.int32)[:, None] * tile_cols_n
        + jnp.arange(tile_cols_n, dtype=jnp.int32)[None, :]
    ).astype(jnp.float32)
    own_taps = jnp.stack(
        [make_taps(geometry, columns[b]) for b in range(count_cols)], axis=1
    )
    own_taps = jnp.broadcast_to(
        own_taps[:, None, :, None], (held, count_rows, count_cols, tiles_here) + own_taps.shape[2:]
    ).reshape((-1,) + own_taps.shape[2:])
    values = interpolate(shifted.reshape(-1, 2, length), own_taps, tile_cols_n)
    count = values.shape[0] // 2
    values = jnp.stack([values[:count], values[count:]], axis=1)
    geo_rows = jnp.broadcast_to(
        geometry[3:5].T[:, None, None, None, :], (held, count_rows, count_cols, tiles_here, 2)
    ).reshape(count, 2)
    extra = jnp.zeros((count, 2, length - tile_cols_n), values.dtype)
    extra = extra.at[:, 0, :2].set(geo_rows)
    message = jnp.concatenate([values, extra], axis=2).reshape(
        held, count_rows, count_cols, tiles_here, 2, length
    )
    message = jnp.transpose(message, (1, 2, 0, 3, 4, 5)).reshape(
        devices_all, held * tiles_here, 2, length
    )
    got = lax.all_to_all(message, ("tx", "ty"), 0, 0, tiled=True)
    got = got.reshape(slots, tiles_here, 2, length)
    tilt = got[:, 0, 0, tile_cols_n]
    base_phase = got[:, 0, 0, tile_cols_n + 1]
    scale = 1.0 / math.sqrt(slots)
    outs = []
    for r in range(tiles_here):
        values = jnp.transpose(got[:, r, :, :tile_cols_n], (1, 0, 2)).reshape(
            2 * slots, tile_cols_n
        )
        rows = (
            row_index * rows_here + r * tile_rows_n + jnp.arange(tile_rows_n, dtype=jnp.int32)
        ).astype(jnp.float32)
        left = phase_matrix(tilt, base_phase, rows)
        product = jnp.dot(left, values, preferred_element_type=jnp.float32).reshape(
            2, tile_rows_n, tile_cols_n
        )
        outs.append(product)
    product = outs[0] if tiles_here == 1 else jnp.concatenate(outs, axis=1)
    return image_in + scale * product


def solution(mesh):
    in_specs = (
        P(("tx", "ty"), None, None),
        P(None, ("tx", "ty")),
        P(("tx", "ty"), None),
        P(None, "tx"),
        P(None, "tx", "ty"),
    )
    out_specs = P(None, "tx", "ty")
    return jax.shard_map(body, mesh=mesh, in_specs=in_specs, out_specs=out_specs, check_vma=False)
```

```python
import math

import jax
import jax.numpy as jnp
from jax import lax
from jax.sharding import PartitionSpec as P

TAPS = 8


def make_taps(geometry, columns):
    rate = geometry[0].astype(jnp.float32)[:, None]
    shift = geometry[1].astype(jnp.float32)[:, None]
    ramp = geometry[2].astype(jnp.float32)[:, None]
    fraction = 0.5 + 0.45 * jnp.sin(rate * columns[None, :] + shift)
    places = jnp.arange(TAPS).astype(jnp.float32)
    spread = places[None, :, None] - 3.0 - fraction[:, None, :]
    angle_x = jnp.pi * spread
    kernel = jnp.sin(angle_x) / angle_x * (0.54 + 0.46 * jnp.cos(angle_x / 4.0))
    turning = ramp * columns[None, :]
    real_part = kernel * jnp.cos(turning)[:, None, :]
    imag_part = kernel * jnp.sin(turning)[:, None, :]
    return jnp.concatenate([real_part, imag_part], axis=1).astype(jnp.bfloat16)


def interpolate(windows, taps, width):
    real_sum = jnp.zeros((windows.shape[0], width), jnp.float32)
    imag_sum = jnp.zeros((windows.shape[0], width), jnp.float32)
    for k in range(TAPS):
        segment = windows[:, :, k : k + width].astype(jnp.float32)
        tap_real = taps[:, k].astype(jnp.float32)
        tap_imag = taps[:, TAPS + k].astype(jnp.float32)
        real_sum = real_sum + tap_real * segment[:, 0] - tap_imag * segment[:, 1]
        imag_sum = imag_sum + tap_real * segment[:, 1] + tap_imag * segment[:, 0]
    return jnp.concatenate([real_sum, imag_sum], axis=0).astype(jnp.bfloat16)


def phase_matrix(tilt, base_phase, rows):
    angles = (
        rows[:, None] * tilt.astype(jnp.float32)[None, :] + base_phase.astype(jnp.float32)[None, :]
    )
    cosine = jnp.cos(angles).astype(jnp.bfloat16)
    sine = jnp.sin(angles).astype(jnp.bfloat16)
    upper = jnp.concatenate([cosine, -sine], axis=1)
    lower = jnp.concatenate([sine, cosine], axis=1)
    return jnp.concatenate([upper, lower], axis=0)


def body(pulses, geometry, footprint, offsets, image_in):
    count_rows = lax.axis_size("tx")
    count_cols = lax.axis_size("ty")
    devices_all = count_rows * count_cols
    held = pulses.shape[0]
    slots = devices_all * held
    tiles_here = offsets.shape[1]
    tiles_all = count_rows * tiles_here
    rows_here = image_in.shape[1]
    tile_rows_n = rows_here // tiles_here
    tile_cols_n = image_in.shape[2]
    length = tile_cols_n + TAPS
    row_index = lax.axis_index("tx")
    col_index = lax.axis_index("ty")

    off_send = offsets.reshape(devices_all, held, tiles_here).astype(jnp.float32)
    geo_send = jnp.broadcast_to(
        geometry.T.astype(jnp.float32)[None], (devices_all, held, 5)
    )
    first = lax.all_to_all(
        jnp.concatenate([off_send, geo_send], axis=2), ("tx", "ty"), 0, 0, tiled=True
    )
    off_got = first[:, :, :tiles_here].reshape(count_rows, count_cols, held, tiles_here)[:, 0]
    mine = jnp.transpose(off_got, (1, 0, 2)).reshape(held, tiles_all).astype(jnp.int32)
    got_geo = first[:, :, tiles_here:].reshape(slots, 5)
    tilt = got_geo[:, 3]
    base_phase = got_geo[:, 4]

    live = jnp.any(
        footprint[:, :, None] == jnp.arange(tiles_all, dtype=jnp.int32)[None, None, :], axis=1
    )

    lanes = 128
    row_count = pulses.shape[2] // lanes
    span = 6
    signal = pulses.reshape(held, 2, row_count, lanes)
    starts = mine.reshape(held, count_rows, 1, tiles_here)
    starts = starts + (jnp.arange(count_cols, dtype=jnp.int32) * tile_cols_n)[None, None, :, None]
    starts = starts.reshape(held, -1)
    lit = jnp.broadcast_to(
        live.reshape(held, count_rows, 1, tiles_here), (held, count_rows, count_cols, tiles_here)
    ).reshape(held, -1)
    first_row = starts // lanes
    shift = starts % lanes
    row_pick = (
        jnp.arange(row_count, dtype=jnp.int32)[None, None, None, :]
        == first_row[:, :, None, None] + jnp.arange(span, dtype=jnp.int32)[None, None, :, None]
    ) & lit[:, :, None, None]
    gathered = jnp.einsum(
        "hwjn,hcnl->hwcjl",
        row_pick.astype(pulses.dtype),
        signal,
        preferred_element_type=jnp.float32,
    ).astype(pulses.dtype)
    paired = jnp.concatenate([gathered[:, :, :, :-1], gathered[:, :, :, 1:]], axis=-1)
    lane_pick = (
        jnp.arange(2 * lanes, dtype=jnp.int32)[None, None, :, None]
        == shift[:, :, None, None] + jnp.arange(lanes, dtype=jnp.int32)[None, None, None, :]
    )
    shifted = jnp.einsum(
        "hwcjm,hwml->hwcjl",
        paired,
        lane_pick.astype(pulses.dtype),
        preferred_element_type=jnp.float32,
    ).astype(pulses.dtype)
    shifted = shifted.reshape(held, count_rows, count_cols, tiles_here, 2, (span - 1) * lanes)
    shifted = shifted[..., :length]

    columns = (
        jnp.arange(count_cols, dtype=jnp.int32)[:, None] * tile_cols_n
        + jnp.arange(tile_cols_n, dtype=jnp.int32)[None, :]
    ).astype(jnp.float32)
    own_taps = jnp.stack(
        [make_taps(geometry, columns[b]) for b in range(count_cols)], axis=1
    )
    own_taps = jnp.broadcast_to(
        own_taps[:, None, :, None], (held, count_rows, count_cols, tiles_here) + own_taps.shape[2:]
    ).reshape((-1,) + own_taps.shape[2:])
    values = interpolate(shifted.reshape(-1, 2, length), own_taps, tile_cols_n)
    count = values.shape[0] // 2
    values = jnp.stack([values[:count], values[count:]], axis=1)
    message = values.reshape(held, count_rows, count_cols, tiles_here, 2, tile_cols_n)
    message = jnp.transpose(message, (1, 2, 0, 3, 4, 5)).reshape(
        devices_all, held * tiles_here, 2, tile_cols_n
    )
    got = lax.all_to_all(message, ("tx", "ty"), 0, 0, tiled=True)
    got = got.reshape(slots, tiles_here, 2, tile_cols_n)
    scale = 1.0 / math.sqrt(slots)
    outs = []
    for r in range(tiles_here):
        values = jnp.transpose(got[:, r], (1, 0, 2)).reshape(
            2 * slots, tile_cols_n
        )
        rows = (
            row_index * rows_here + r * tile_rows_n + jnp.arange(tile_rows_n, dtype=jnp.int32)
        ).astype(jnp.float32)
        left = phase_matrix(tilt, base_phase, rows)
        product = jnp.dot(left, values, preferred_element_type=jnp.float32).reshape(
            2, tile_rows_n, tile_cols_n
        )
        outs.append(product)
    product = outs[0] if tiles_here == 1 else jnp.concatenate(outs, axis=1)
    return image_in + scale * product


def solution(mesh):
    in_specs = (
        P(("tx", "ty"), None, None),
        P(None, ("tx", "ty")),
        P(("tx", "ty"), None),
        P(None, "tx"),
        P(None, "tx", "ty"),
    )
    out_specs = P(None, "tx", "ty")
    return jax.shard_map(body, mesh=mesh, in_specs=in_specs, out_specs=out_specs, check_vma=False)
```

```python
import math

import jax
import jax.numpy as jnp
from jax import lax
from jax.experimental import pallas as pl
from jax.experimental.pallas import tpu as pltpu
from jax.sharding import PartitionSpec as P

TAPS = 8


def make_taps(geometry, columns):
    rate = geometry[0].astype(jnp.float32)[:, None]
    shift = geometry[1].astype(jnp.float32)[:, None]
    ramp = geometry[2].astype(jnp.float32)[:, None]
    fraction = 0.5 + 0.45 * jnp.sin(rate * columns[None, :] + shift)
    places = jnp.arange(TAPS).astype(jnp.float32)
    spread = places[None, :, None] - 3.0 - fraction[:, None, :]
    angle_x = jnp.pi * spread
    kernel = jnp.sin(angle_x) / angle_x * (0.54 + 0.46 * jnp.cos(angle_x / 4.0))
    turning = ramp * columns[None, :]
    real_part = kernel * jnp.cos(turning)[:, None, :]
    imag_part = kernel * jnp.sin(turning)[:, None, :]
    return jnp.concatenate([real_part, imag_part], axis=1).astype(jnp.bfloat16)


def interpolate(windows, taps, width):
    real_sum = jnp.zeros((windows.shape[0], width), jnp.float32)
    imag_sum = jnp.zeros((windows.shape[0], width), jnp.float32)
    for k in range(TAPS):
        segment = windows[:, :, k : k + width].astype(jnp.float32)
        tap_real = taps[:, k].astype(jnp.float32)
        tap_imag = taps[:, TAPS + k].astype(jnp.float32)
        real_sum = real_sum + tap_real * segment[:, 0] - tap_imag * segment[:, 1]
        imag_sum = imag_sum + tap_real * segment[:, 1] + tap_imag * segment[:, 0]
    return jnp.concatenate([real_sum, imag_sum], axis=0).astype(jnp.bfloat16)


def phase_matrix(tilt, base_phase, rows):
    angles = (
        rows[:, None] * tilt.astype(jnp.float32)[None, :] + base_phase.astype(jnp.float32)[None, :]
    )
    cosine = jnp.cos(angles).astype(jnp.bfloat16)
    sine = jnp.sin(angles).astype(jnp.bfloat16)
    upper = jnp.concatenate([cosine, -sine], axis=1)
    lower = jnp.concatenate([sine, cosine], axis=1)
    return jnp.concatenate([upper, lower], axis=0)


def cut_and_interpolate(starts, lit, pulses, taps, held, count_cols, tiles_here, width):
    count = starts.shape[0]
    samples = pulses.shape[2]
    chunk = 768

    def kernel(starts_ref, lit_ref, pulses_ref, taps_ref, out_ref):
        def step(o, carry):
            h = (o // tiles_here) % held
            b = (o // (tiles_here * held)) % count_cols
            start = starts_ref[o]
            base = jnp.minimum((start // 128) * 128, samples - chunk)
            s = start - base
            x = pulses_ref[h, :, pl.ds(pl.multiple_of(base, 128), chunk)].astype(jnp.float32)
            both = jnp.concatenate([x, x[1:2], x[0:1]], axis=0)
            acc = jnp.zeros((4, width), jnp.float32)
            for k in range(TAPS):
                seg = pltpu.roll(both, (chunk - s - k) % chunk, 1)[:, :width]
                acc = acc + taps_ref[h, b, k] * seg
            res = acc[0:2] + acc[2:4]
            res = jnp.where(lit_ref[o] != 0, res, jnp.zeros_like(res))
            out_ref[o] = res.astype(out_ref.dtype)
            return carry

        lax.fori_loop(0, count, step, 0)

    return pl.pallas_call(
        kernel,
        out_shape=jax.ShapeDtypeStruct((count, 2, width), pulses.dtype),
        grid_spec=pltpu.PrefetchScalarGridSpec(
            num_scalar_prefetch=2,
            grid=(1,),
            in_specs=[
                pl.BlockSpec(pulses.shape, lambda i, *_: (0, 0, 0)),
                pl.BlockSpec(taps.shape, lambda i, *_: (0, 0, 0, 0, 0)),
            ],
            out_specs=pl.BlockSpec((count, 2, width), lambda i, *_: (0, 0, 0)),
        ),
    )(starts, lit, pulses, taps)


def body(pulses, geometry, footprint, offsets, image_in):
    count_rows = lax.axis_size("tx")
    count_cols = lax.axis_size("ty")
    devices_all = count_rows * count_cols
    held = pulses.shape[0]
    slots = devices_all * held
    tiles_here = offsets.shape[1]
    tiles_all = count_rows * tiles_here
    rows_here = image_in.shape[1]
    tile_rows_n = rows_here // tiles_here
    tile_cols_n = image_in.shape[2]
    length = tile_cols_n + TAPS
    row_index = lax.axis_index("tx")
    col_index = lax.axis_index("ty")

    off_send = offsets.reshape(devices_all, held, tiles_here).astype(jnp.float32)
    geo_send = jnp.broadcast_to(
        geometry.T.astype(jnp.float32)[None], (devices_all, held, 5)
    )
    first = lax.all_to_all(
        jnp.concatenate([off_send, geo_send], axis=2), ("tx", "ty"), 0, 0, tiled=True
    )
    off_got = first[:, :, :tiles_here].reshape(count_rows, count_cols, held, tiles_here)[:, 0]
    mine = jnp.transpose(off_got, (1, 0, 2)).reshape(held, tiles_all).astype(jnp.int32)
    got_geo = first[:, :, tiles_here:].reshape(slots, 5)
    tilt = got_geo[:, 3]
    base_phase = got_geo[:, 4]

    live = jnp.any(
        footprint[:, :, None] == jnp.arange(tiles_all, dtype=jnp.int32)[None, None, :], axis=1
    )

    starts = jnp.transpose(mine.reshape(held, count_rows, 1, tiles_here), (1, 2, 0, 3))
    starts = starts + (jnp.arange(count_cols, dtype=jnp.int32) * tile_cols_n)[None, :, None, None]
    lit = jnp.broadcast_to(
        jnp.transpose(live.reshape(held, count_rows, 1, tiles_here), (1, 2, 0, 3)),
        (count_rows, count_cols, held, tiles_here),
    ).astype(jnp.int32)
    columns = (
        jnp.arange(count_cols, dtype=jnp.int32)[:, None] * tile_cols_n
        + jnp.arange(tile_cols_n, dtype=jnp.int32)[None, :]
    ).astype(jnp.float32)
    own_taps = jnp.stack(
        [make_taps(geometry, columns[b]) for b in range(count_cols)], axis=1
    ).astype(jnp.float32)
    tap_real = own_taps[:, :, :TAPS]
    tap_imag = own_taps[:, :, TAPS:]
    tap_rows = jnp.stack([tap_real, tap_real, -tap_imag, tap_imag], axis=3)
    values = cut_and_interpolate(
        starts.reshape(-1), lit.reshape(-1), pulses, tap_rows, held, count_cols, tiles_here,
        tile_cols_n,
    )
    message = values.reshape(devices_all, held * tiles_here, 2, tile_cols_n)
    got = lax.all_to_all(message, ("tx", "ty"), 0, 0, tiled=True)
    got = got.reshape(slots, tiles_here, 2, tile_cols_n)
    scale = 1.0 / math.sqrt(slots)
    outs = []
    for r in range(tiles_here):
        values = jnp.transpose(got[:, r], (1, 0, 2)).reshape(
            2 * slots, tile_cols_n
        )
        rows = (
            row_index * rows_here + r * tile_rows_n + jnp.arange(tile_rows_n, dtype=jnp.int32)
        ).astype(jnp.float32)
        left = phase_matrix(tilt, base_phase, rows)
        product = jnp.dot(left, values, preferred_element_type=jnp.float32).reshape(
            2, tile_rows_n, tile_cols_n
        )
        outs.append(product)
    product = outs[0] if tiles_here == 1 else jnp.concatenate(outs, axis=1)
    return image_in + scale * product


def solution(mesh):
    in_specs = (
        P(("tx", "ty"), None, None),
        P(None, ("tx", "ty")),
        P(("tx", "ty"), None),
        P(None, "tx"),
        P(None, "tx", "ty"),
    )
    out_specs = P(None, "tx", "ty")
    return jax.shard_map(body, mesh=mesh, in_specs=in_specs, out_specs=out_specs, check_vma=False)
```

```python
import math

import jax
import jax.numpy as jnp
from jax import lax
from jax.sharding import PartitionSpec as P

TAPS = 8


def make_taps(geometry, columns):
    rate = geometry[0].astype(jnp.float32)[:, None]
    shift = geometry[1].astype(jnp.float32)[:, None]
    ramp = geometry[2].astype(jnp.float32)[:, None]
    fraction = 0.5 + 0.45 * jnp.sin(rate * columns[None, :] + shift)
    places = jnp.arange(TAPS).astype(jnp.float32)
    spread = places[None, :, None] - 3.0 - fraction[:, None, :]
    angle_x = jnp.pi * spread
    kernel = jnp.sin(angle_x) / angle_x * (0.54 + 0.46 * jnp.cos(angle_x / 4.0))
    turning = ramp * columns[None, :]
    real_part = kernel * jnp.cos(turning)[:, None, :]
    imag_part = kernel * jnp.sin(turning)[:, None, :]
    return jnp.concatenate([real_part, imag_part], axis=1).astype(jnp.bfloat16)


def interpolate(windows, taps, width):
    real_sum = jnp.zeros((windows.shape[0], width), jnp.float32)
    imag_sum = jnp.zeros((windows.shape[0], width), jnp.float32)
    for k in range(TAPS):
        segment = windows[:, :, k : k + width].astype(jnp.float32)
        tap_real = taps[:, k].astype(jnp.float32)
        tap_imag = taps[:, TAPS + k].astype(jnp.float32)
        real_sum = real_sum + tap_real * segment[:, 0] - tap_imag * segment[:, 1]
        imag_sum = imag_sum + tap_real * segment[:, 1] + tap_imag * segment[:, 0]
    return jnp.concatenate([real_sum, imag_sum], axis=0).astype(jnp.bfloat16)


def phase_matrix(tilt, base_phase, rows):
    angles = (
        rows[:, None] * tilt.astype(jnp.float32)[None, :] + base_phase.astype(jnp.float32)[None, :]
    )
    cosine = jnp.cos(angles).astype(jnp.bfloat16)
    sine = jnp.sin(angles).astype(jnp.bfloat16)
    upper = jnp.concatenate([cosine, -sine], axis=1)
    lower = jnp.concatenate([sine, cosine], axis=1)
    return jnp.concatenate([upper, lower], axis=0)


def body(pulses, geometry, footprint, offsets, image_in):
    count_rows = lax.axis_size("tx")
    count_cols = lax.axis_size("ty")
    devices_all = count_rows * count_cols
    held = pulses.shape[0]
    slots = devices_all * held
    tiles_here = offsets.shape[1]
    tiles_all = count_rows * tiles_here
    rows_here = image_in.shape[1]
    tile_rows_n = rows_here // tiles_here
    tile_cols_n = image_in.shape[2]
    length = tile_cols_n + TAPS
    row_index = lax.axis_index("tx")
    col_index = lax.axis_index("ty")

    send_first = jnp.concatenate(
        [
            offsets.astype(jnp.float32).reshape(devices_all, held * tiles_here),
            jnp.broadcast_to(
                geometry.T.astype(jnp.float32).reshape(1, held * 5), (devices_all, held * 5)
            ),
        ],
        axis=1,
    )
    first = lax.all_to_all(send_first, ("tx", "ty"), 0, 0, tiled=True)
    first_off = first[:, : held * tiles_here].reshape(count_rows, count_cols, held, tiles_here)
    mine = jnp.transpose(first_off[:, 0], (1, 0, 2)).reshape(held, tiles_all).astype(jnp.int32)
    got_geo = first[:, held * tiles_here :].reshape(slots, 5)
    tilt = got_geo[:, 3]
    base_phase = got_geo[:, 4]

    live = jnp.any(
        footprint[:, :, None] == jnp.arange(tiles_all, dtype=jnp.int32)[None, None, :], axis=1
    )

    lanes = 128
    row_count = pulses.shape[2] // lanes
    span = 6
    signal = pulses.reshape(held, 2, row_count, lanes)
    starts = mine.reshape(held, count_rows, 1, tiles_here)
    starts = starts + (jnp.arange(count_cols, dtype=jnp.int32) * tile_cols_n)[None, None, :, None]
    starts = starts.reshape(held, -1)
    lit = jnp.broadcast_to(
        live.reshape(held, count_rows, 1, tiles_here), (held, count_rows, count_cols, tiles_here)
    ).reshape(held, -1)
    first_row = starts // lanes
    shift = starts % lanes
    pairs = jnp.concatenate(
        [signal, jnp.concatenate([signal[:, :, 1:], jnp.zeros_like(signal[:, :, :1])], axis=2)],
        axis=-1,
    )
    row_pick = (
        jnp.arange(row_count, dtype=jnp.int32)[None, None, None, :]
        == first_row[:, :, None, None] + jnp.arange(span - 1, dtype=jnp.int32)[None, None, :, None]
    ) & lit[:, :, None, None]
    paired = jnp.einsum(
        "hwjn,hcnl->hwcjl",
        row_pick.astype(pulses.dtype),
        pairs,
        preferred_element_type=jnp.float32,
    ).astype(pulses.dtype)
    lane_pick = (
        jnp.arange(2 * lanes, dtype=jnp.int32)[None, None, :, None]
        == shift[:, :, None, None] + jnp.arange(lanes, dtype=jnp.int32)[None, None, None, :]
    )
    shifted = jnp.einsum(
        "hwcjm,hwml->hwcjl",
        paired,
        lane_pick.astype(pulses.dtype),
        preferred_element_type=jnp.float32,
    ).astype(pulses.dtype)
    shifted = shifted.reshape(held, count_rows, count_cols, tiles_here, 2, (span - 1) * lanes)
    shifted = shifted[..., :length]

    columns = (
        jnp.arange(count_cols, dtype=jnp.int32)[:, None] * tile_cols_n
        + jnp.arange(tile_cols_n, dtype=jnp.int32)[None, :]
    ).astype(jnp.float32)
    own_taps = jnp.stack(
        [make_taps(geometry, columns[b]) for b in range(count_cols)], axis=1
    )
    own_taps = jnp.broadcast_to(
        own_taps[:, None, :, None], (held, count_rows, count_cols, tiles_here) + own_taps.shape[2:]
    ).reshape((-1,) + own_taps.shape[2:])
    windows = shifted.reshape(-1, 2, length)
    real_sum = jnp.zeros((windows.shape[0], tile_cols_n), jnp.float32)
    imag_sum = jnp.zeros((windows.shape[0], tile_cols_n), jnp.float32)
    for k in range(TAPS):
        segment = windows[:, :, k : k + tile_cols_n].astype(jnp.float32)
        tap_real = own_taps[:, k].astype(jnp.float32)
        tap_imag = own_taps[:, TAPS + k].astype(jnp.float32)
        real_sum = real_sum + tap_real * segment[:, 0] - tap_imag * segment[:, 1]
        imag_sum = imag_sum + tap_real * segment[:, 1] + tap_imag * segment[:, 0]
    values = jnp.stack([real_sum, imag_sum], axis=1).astype(jnp.bfloat16)
    message = values.reshape(held, count_rows, count_cols, tiles_here, 2, tile_cols_n)
    message = jnp.transpose(message, (1, 2, 0, 3, 4, 5)).reshape(
        devices_all, held * tiles_here, 2, tile_cols_n
    )
    got = lax.all_to_all(message, ("tx", "ty"), 0, 0, tiled=True)
    got = got.reshape(slots, tiles_here, 2, tile_cols_n)
    scale = 1.0 / math.sqrt(slots)
    outs = []
    for r in range(tiles_here):
        values = jnp.transpose(got[:, r], (1, 0, 2)).reshape(
            2 * slots, tile_cols_n
        )
        rows = (
            row_index * rows_here + r * tile_rows_n + jnp.arange(tile_rows_n, dtype=jnp.int32)
        ).astype(jnp.float32)
        left = phase_matrix(tilt, base_phase, rows)
        product = jnp.dot(left, values, preferred_element_type=jnp.float32).reshape(
            2, tile_rows_n, tile_cols_n
        )
        outs.append(product)
    product = outs[0] if tiles_here == 1 else jnp.concatenate(outs, axis=1)
    return image_in + scale * product


def solution(mesh):
    in_specs = (
        P(("tx", "ty"), None, None),
        P(None, ("tx", "ty")),
        P(("tx", "ty"), None),
        P(None, "tx"),
        P(None, "tx", "ty"),
    )
    out_specs = P(None, "tx", "ty")
    return jax.shard_map(body, mesh=mesh, in_specs=in_specs, out_specs=out_specs, check_vma=False)
```

```python
import math

import jax
import jax.numpy as jnp
from jax import lax
from jax.sharding import PartitionSpec as P

TAPS = 8


def make_taps(geometry, columns):
    rate = geometry[0].astype(jnp.float32)[:, None]
    shift = geometry[1].astype(jnp.float32)[:, None]
    ramp = geometry[2].astype(jnp.float32)[:, None]
    fraction = 0.5 + 0.45 * jnp.sin(rate * columns[None, :] + shift)
    places = jnp.arange(TAPS).astype(jnp.float32)
    spread = places[None, :, None] - 3.0 - fraction[:, None, :]
    angle_x = jnp.pi * spread
    kernel = jnp.sin(angle_x) / angle_x * (0.54 + 0.46 * jnp.cos(angle_x / 4.0))
    turning = ramp * columns[None, :]
    real_part = kernel * jnp.cos(turning)[:, None, :]
    imag_part = kernel * jnp.sin(turning)[:, None, :]
    return jnp.concatenate([real_part, imag_part], axis=1).astype(jnp.bfloat16)


def taps_from_terms(rate_col, shift, turning):
    fraction = 0.5 + 0.45 * jnp.sin(rate_col + shift)
    places = jnp.arange(TAPS).astype(jnp.float32)
    spread = places[None, :, None] - 3.0 - fraction[:, None, :]
    angle_x = jnp.pi * spread
    kernel = jnp.sin(angle_x) / angle_x * (0.54 + 0.46 * jnp.cos(angle_x / 4.0))
    real_part = kernel * jnp.cos(turning)[:, None, :]
    imag_part = kernel * jnp.sin(turning)[:, None, :]
    return jnp.concatenate([real_part, imag_part], axis=1).astype(jnp.bfloat16)


def interpolate(windows, taps, width):
    real_sum = jnp.zeros((windows.shape[0], width), jnp.float32)
    imag_sum = jnp.zeros((windows.shape[0], width), jnp.float32)
    for k in range(TAPS):
        segment = windows[:, :, k : k + width].astype(jnp.float32)
        tap_real = taps[:, k].astype(jnp.float32)
        tap_imag = taps[:, TAPS + k].astype(jnp.float32)
        real_sum = real_sum + tap_real * segment[:, 0] - tap_imag * segment[:, 1]
        imag_sum = imag_sum + tap_real * segment[:, 1] + tap_imag * segment[:, 0]
    return jnp.concatenate([real_sum, imag_sum], axis=0).astype(jnp.bfloat16)


def phase_matrix(tilt, base_phase, rows):
    angles = (
        rows[:, None] * tilt.astype(jnp.float32)[None, :] + base_phase.astype(jnp.float32)[None, :]
    )
    cosine = jnp.cos(angles).astype(jnp.bfloat16)
    sine = jnp.sin(angles).astype(jnp.bfloat16)
    upper = jnp.concatenate([cosine, -sine], axis=1)
    lower = jnp.concatenate([sine, cosine], axis=1)
    return jnp.concatenate([upper, lower], axis=0)


def body(pulses, geometry, footprint, offsets, image_in):
    count_rows = lax.axis_size("tx")
    count_cols = lax.axis_size("ty")
    devices_all = count_rows * count_cols
    held = pulses.shape[0]
    slots = devices_all * held
    tiles_here = offsets.shape[1]
    tiles_all = count_rows * tiles_here
    rows_here = image_in.shape[1]
    tile_rows_n = rows_here // tiles_here
    tile_cols_n = image_in.shape[2]
    length = tile_cols_n + TAPS
    row_index = lax.axis_index("tx")
    col_index = lax.axis_index("ty")

    send_first = jnp.concatenate(
        [
            offsets.astype(jnp.float32).reshape(devices_all, held * tiles_here),
            jnp.broadcast_to(
                geometry.T.astype(jnp.float32).reshape(1, held * 5), (devices_all, held * 5)
            ),
        ],
        axis=1,
    )
    first = lax.all_to_all(send_first, ("tx", "ty"), 0, 0, tiled=True)
    first_off = first[:, : held * tiles_here].reshape(count_rows, count_cols, held, tiles_here)
    mine = jnp.transpose(first_off[:, 0], (1, 0, 2)).reshape(held, tiles_all).astype(jnp.int32)
    got_geo = first[:, held * tiles_here :].reshape(slots, 5)
    tilt = got_geo[:, 3]
    base_phase = got_geo[:, 4]

    live = jnp.any(
        footprint[:, :, None] == jnp.arange(tiles_all, dtype=jnp.int32)[None, None, :], axis=1
    )

    lanes = 128
    row_count = pulses.shape[2] // lanes
    span = 6
    signal = pulses.reshape(held, 2, row_count, lanes)
    starts = mine.reshape(held, count_rows, 1, tiles_here)
    starts = starts + (jnp.arange(count_cols, dtype=jnp.int32) * tile_cols_n)[None, None, :, None]
    starts = starts.reshape(held, -1)
    lit = jnp.broadcast_to(
        live.reshape(held, count_rows, 1, tiles_here), (held, count_rows, count_cols, tiles_here)
    ).reshape(held, -1)
    first_row = starts // lanes
    shift = starts % lanes
    pairs = jnp.concatenate(
        [signal, jnp.concatenate([signal[:, :, 1:], jnp.zeros_like(signal[:, :, :1])], axis=2)],
        axis=-1,
    )
    row_pick = (
        jnp.arange(row_count, dtype=jnp.int32)[None, None, None, :]
        == first_row[:, :, None, None] + jnp.arange(span - 1, dtype=jnp.int32)[None, None, :, None]
    ) & lit[:, :, None, None]
    paired = jnp.einsum(
        "hwjn,hcnl->hwcjl",
        row_pick.astype(pulses.dtype),
        pairs,
        preferred_element_type=jnp.float32,
    ).astype(pulses.dtype)
    lane_pick = (
        jnp.arange(2 * lanes, dtype=jnp.int32)[None, None, :, None]
        == shift[:, :, None, None] + jnp.arange(lanes, dtype=jnp.int32)[None, None, None, :]
    )
    shifted = jnp.einsum(
        "hwcjm,hwml->hwcjl",
        paired,
        lane_pick.astype(pulses.dtype),
        preferred_element_type=jnp.float32,
    ).astype(pulses.dtype)
    shifted = shifted.reshape(held, count_rows, count_cols, tiles_here, 2, (span - 1) * lanes)
    shifted = shifted[..., :length]

    span_cols = count_cols * tile_cols_n
    columns = jnp.arange(span_cols, dtype=jnp.int32).astype(jnp.float32)
    zero = jnp.zeros((span_cols,), jnp.float32)
    one = jnp.ones((span_cols,), jnp.float32)
    basis = jnp.stack(
        [
            jnp.concatenate([columns, zero, zero]),
            jnp.concatenate([zero, one, zero]),
            jnp.concatenate([zero, zero, columns]),
            jnp.concatenate([zero, zero, zero]),
            jnp.concatenate([zero, zero, zero]),
        ]
    )
    terms = jnp.dot(
        geometry.T.astype(jnp.float32), basis, precision=lax.Precision.HIGHEST,
        preferred_element_type=jnp.float32,
    )
    own_taps = taps_from_terms(
        terms[:, :span_cols], terms[:, span_cols : 2 * span_cols], terms[:, 2 * span_cols :]
    )
    own_taps = own_taps.reshape(held, TAPS * 2, count_cols, tile_cols_n).transpose(0, 2, 1, 3)
    own_taps = jnp.broadcast_to(
        own_taps[:, None, :, None], (held, count_rows, count_cols, tiles_here) + own_taps.shape[2:]
    ).reshape((-1,) + own_taps.shape[2:])
    windows = shifted.reshape(-1, 2, length)
    real_sum = jnp.zeros((windows.shape[0], tile_cols_n), jnp.float32)
    imag_sum = jnp.zeros((windows.shape[0], tile_cols_n), jnp.float32)
    for k in range(TAPS):
        segment = windows[:, :, k : k + tile_cols_n].astype(jnp.float32)
        tap_real = own_taps[:, k].astype(jnp.float32)
        tap_imag = own_taps[:, TAPS + k].astype(jnp.float32)
        real_sum = real_sum + tap_real * segment[:, 0] - tap_imag * segment[:, 1]
        imag_sum = imag_sum + tap_real * segment[:, 1] + tap_imag * segment[:, 0]
    values = jnp.stack([real_sum, imag_sum], axis=1).astype(jnp.bfloat16)
    message = values.reshape(held, count_rows, count_cols, tiles_here, 2, tile_cols_n)
    message = jnp.transpose(message, (1, 2, 0, 3, 4, 5)).reshape(
        devices_all, held * tiles_here, 2, tile_cols_n
    )
    got = lax.all_to_all(message, ("tx", "ty"), 0, 0, tiled=True)
    got = got.reshape(slots, tiles_here, 2, tile_cols_n)
    scale = 1.0 / math.sqrt(slots)
    outs = []
    for r in range(tiles_here):
        values = jnp.transpose(got[:, r], (1, 0, 2)).reshape(
            2 * slots, tile_cols_n
        )
        rows = (
            row_index * rows_here + r * tile_rows_n + jnp.arange(tile_rows_n, dtype=jnp.int32)
        ).astype(jnp.float32)
        left = phase_matrix(tilt, base_phase, rows)
        product = jnp.dot(left, values, preferred_element_type=jnp.float32).reshape(
            2, tile_rows_n, tile_cols_n
        )
        outs.append(product)
    product = outs[0] if tiles_here == 1 else jnp.concatenate(outs, axis=1)
    return image_in + scale * product


def solution(mesh):
    in_specs = (
        P(("tx", "ty"), None, None),
        P(None, ("tx", "ty")),
        P(("tx", "ty"), None),
        P(None, "tx"),
        P(None, "tx", "ty"),
    )
    out_specs = P(None, "tx", "ty")
    return jax.shard_map(body, mesh=mesh, in_specs=in_specs, out_specs=out_specs, check_vma=False)
```

```python
import math

import jax
import jax.numpy as jnp
from jax import lax
from jax.sharding import PartitionSpec as P

TAPS = 8


def make_taps(geometry, columns):
    rate = geometry[0].astype(jnp.float32)[:, None]
    shift = geometry[1].astype(jnp.float32)[:, None]
    ramp = geometry[2].astype(jnp.float32)[:, None]
    fraction = 0.5 + 0.45 * jnp.sin(rate * columns[None, :] + shift)
    places = jnp.arange(TAPS).astype(jnp.float32)
    spread = places[None, :, None] - 3.0 - fraction[:, None, :]
    angle_x = jnp.pi * spread
    kernel = jnp.sin(angle_x) / angle_x * (0.54 + 0.46 * jnp.cos(angle_x / 4.0))
    turning = ramp * columns[None, :]
    real_part = kernel * jnp.cos(turning)[:, None, :]
    imag_part = kernel * jnp.sin(turning)[:, None, :]
    return jnp.concatenate([real_part, imag_part], axis=1).astype(jnp.bfloat16)


def taps_from_terms(rate_col, shift, turning):
    fraction = 0.5 + 0.45 * jnp.sin(rate_col + shift)
    places = jnp.arange(TAPS).astype(jnp.float32)
    spread = places[None, :, None] - 3.0 - fraction[:, None, :]
    angle_x = jnp.pi * spread
    kernel = jnp.sin(angle_x) / angle_x * (0.54 + 0.46 * jnp.cos(angle_x / 4.0))
    real_part = kernel * jnp.cos(turning)[:, None, :]
    imag_part = kernel * jnp.sin(turning)[:, None, :]
    return jnp.concatenate([real_part, imag_part], axis=1).astype(jnp.bfloat16)


def interpolate(windows, taps, width):
    real_sum = jnp.zeros((windows.shape[0], width), jnp.float32)
    imag_sum = jnp.zeros((windows.shape[0], width), jnp.float32)
    for k in range(TAPS):
        segment = windows[:, :, k : k + width].astype(jnp.float32)
        tap_real = taps[:, k].astype(jnp.float32)
        tap_imag = taps[:, TAPS + k].astype(jnp.float32)
        real_sum = real_sum + tap_real * segment[:, 0] - tap_imag * segment[:, 1]
        imag_sum = imag_sum + tap_real * segment[:, 1] + tap_imag * segment[:, 0]
    return jnp.concatenate([real_sum, imag_sum], axis=0).astype(jnp.bfloat16)


def phase_matrix(tilt, base_phase, rows):
    angles = (
        rows[:, None] * tilt.astype(jnp.float32)[None, :] + base_phase.astype(jnp.float32)[None, :]
    )
    cosine = jnp.cos(angles).astype(jnp.bfloat16)
    sine = jnp.sin(angles).astype(jnp.bfloat16)
    upper = jnp.concatenate([cosine, -sine], axis=1)
    lower = jnp.concatenate([sine, cosine], axis=1)
    return jnp.concatenate([upper, lower], axis=0)


def body(pulses, geometry, footprint, offsets, image_in):
    count_rows = lax.axis_size("tx")
    count_cols = lax.axis_size("ty")
    devices_all = count_rows * count_cols
    held = pulses.shape[0]
    slots = devices_all * held
    tiles_here = offsets.shape[1]
    tiles_all = count_rows * tiles_here
    rows_here = image_in.shape[1]
    tile_rows_n = rows_here // tiles_here
    tile_cols_n = image_in.shape[2]
    length = tile_cols_n + TAPS
    row_index = lax.axis_index("tx")
    col_index = lax.axis_index("ty")

    send_first = jnp.concatenate(
        [
            (offsets.astype(jnp.float32) + (col_index * tile_cols_n).astype(jnp.float32)).reshape(
                devices_all, held * tiles_here
            ),
            jnp.broadcast_to(
                geometry.T.astype(jnp.float32).reshape(1, held * 5), (devices_all, held * 5)
            ),
        ],
        axis=1,
    )
    first = lax.all_to_all(send_first, ("tx", "ty"), 0, 0, tiled=True)
    starts = jnp.transpose(
        first[:, : held * tiles_here].reshape(devices_all, held, tiles_here), (1, 0, 2)
    ).reshape(held, -1).astype(jnp.int32)
    got_geo = first[:, held * tiles_here :].reshape(slots, 5)
    tilt = got_geo[:, 3]
    base_phase = got_geo[:, 4]

    live = jnp.any(
        footprint[:, :, None] == jnp.arange(tiles_all, dtype=jnp.int32)[None, None, :], axis=1
    )

    lanes = 128
    row_count = pulses.shape[2] // lanes
    span = 6
    signal = pulses.reshape(held, 2, row_count, lanes)
    lit = jnp.broadcast_to(
        live.reshape(held, count_rows, 1, tiles_here), (held, count_rows, count_cols, tiles_here)
    ).reshape(held, -1)
    first_row = starts // lanes
    shift = starts % lanes
    pairs = jnp.concatenate(
        [signal, jnp.concatenate([signal[:, :, 1:], jnp.zeros_like(signal[:, :, :1])], axis=2)],
        axis=-1,
    )
    row_pick = (
        jnp.arange(row_count, dtype=jnp.int32)[None, None, None, :]
        == first_row[:, :, None, None] + jnp.arange(span - 1, dtype=jnp.int32)[None, None, :, None]
    ) & lit[:, :, None, None]
    paired = jnp.einsum(
        "hwjn,hcnl->hwcjl",
        row_pick.astype(pulses.dtype),
        pairs,
        preferred_element_type=jnp.float32,
    ).astype(pulses.dtype)
    lane_pick = (
        jnp.arange(2 * lanes, dtype=jnp.int32)[None, None, :, None]
        == shift[:, :, None, None] + jnp.arange(lanes, dtype=jnp.int32)[None, None, None, :]
    )
    shifted = jnp.einsum(
        "hwcjm,hwml->hwcjl",
        paired,
        lane_pick.astype(pulses.dtype),
        preferred_element_type=jnp.float32,
    ).astype(pulses.dtype)
    shifted = shifted.reshape(held, count_rows, count_cols, tiles_here, 2, (span - 1) * lanes)
    shifted = shifted[..., :length]

    span_cols = count_cols * tile_cols_n
    columns = jnp.arange(span_cols, dtype=jnp.int32).astype(jnp.float32)
    zero = jnp.zeros((span_cols,), jnp.float32)
    one = jnp.ones((span_cols,), jnp.float32)
    basis = jnp.stack(
        [
            jnp.concatenate([columns, zero, zero]),
            jnp.concatenate([zero, one, zero]),
            jnp.concatenate([zero, zero, columns]),
            jnp.concatenate([zero, zero, zero]),
            jnp.concatenate([zero, zero, zero]),
        ]
    )
    terms = jnp.dot(
        geometry.T.astype(jnp.float32), basis, precision=lax.Precision.HIGHEST,
        preferred_element_type=jnp.float32,
    )
    own_taps = taps_from_terms(
        terms[:, :span_cols], terms[:, span_cols : 2 * span_cols], terms[:, 2 * span_cols :]
    )
    own_taps = own_taps.reshape(held, TAPS * 2, count_cols, tile_cols_n).transpose(0, 2, 1, 3)
    own_taps = jnp.broadcast_to(
        own_taps[:, None, :, None], (held, count_rows, count_cols, tiles_here) + own_taps.shape[2:]
    ).reshape((-1,) + own_taps.shape[2:])
    windows = shifted.reshape(-1, 2, length)
    real_sum = jnp.zeros((windows.shape[0], tile_cols_n), jnp.float32)
    imag_sum = jnp.zeros((windows.shape[0], tile_cols_n), jnp.float32)
    for k in range(TAPS):
        segment = windows[:, :, k : k + tile_cols_n].astype(jnp.float32)
        tap_real = own_taps[:, k].astype(jnp.float32)
        tap_imag = own_taps[:, TAPS + k].astype(jnp.float32)
        real_sum = real_sum + tap_real * segment[:, 0] - tap_imag * segment[:, 1]
        imag_sum = imag_sum + tap_real * segment[:, 1] + tap_imag * segment[:, 0]
    values = jnp.stack([real_sum, imag_sum], axis=1).astype(jnp.bfloat16)
    message = values.reshape(held, count_rows, count_cols, tiles_here, 2, tile_cols_n)
    message = jnp.transpose(message, (1, 2, 0, 3, 4, 5)).reshape(
        devices_all, held * tiles_here, 2, tile_cols_n
    )
    got = lax.all_to_all(message, ("tx", "ty"), 0, 0, tiled=True)
    got = got.reshape(slots, tiles_here, 2, tile_cols_n)
    scale = 1.0 / math.sqrt(slots)
    outs = []
    for r in range(tiles_here):
        values = jnp.transpose(got[:, r], (1, 0, 2)).reshape(
            2 * slots, tile_cols_n
        )
        rows = (
            row_index * rows_here + r * tile_rows_n + jnp.arange(tile_rows_n, dtype=jnp.int32)
        ).astype(jnp.float32)
        left = phase_matrix(tilt, base_phase, rows)
        product = jnp.dot(left, values, preferred_element_type=jnp.float32).reshape(
            2, tile_rows_n, tile_cols_n
        )
        outs.append(product)
    product = outs[0] if tiles_here == 1 else jnp.concatenate(outs, axis=1)
    return image_in + scale * product


def solution(mesh):
    in_specs = (
        P(("tx", "ty"), None, None),
        P(None, ("tx", "ty")),
        P(("tx", "ty"), None),
        P(None, "tx"),
        P(None, "tx", "ty"),
    )
    out_specs = P(None, "tx", "ty")
    return jax.shard_map(body, mesh=mesh, in_specs=in_specs, out_specs=out_specs, check_vma=False)
```

```python
import math

import jax
import jax.numpy as jnp
from jax import lax
from jax.sharding import PartitionSpec as P

TAPS = 8


def make_taps(geometry, columns):
    rate = geometry[0].astype(jnp.float32)[:, None]
    shift = geometry[1].astype(jnp.float32)[:, None]
    ramp = geometry[2].astype(jnp.float32)[:, None]
    fraction = 0.5 + 0.45 * jnp.sin(rate * columns[None, :] + shift)
    places = jnp.arange(TAPS).astype(jnp.float32)
    spread = places[None, :, None] - 3.0 - fraction[:, None, :]
    angle_x = jnp.pi * spread
    kernel = jnp.sin(angle_x) / angle_x * (0.54 + 0.46 * jnp.cos(angle_x / 4.0))
    turning = ramp * columns[None, :]
    real_part = kernel * jnp.cos(turning)[:, None, :]
    imag_part = kernel * jnp.sin(turning)[:, None, :]
    return jnp.concatenate([real_part, imag_part], axis=1).astype(jnp.bfloat16)


def taps_from_terms(rate_col, shift, turning):
    fraction = 0.5 + 0.45 * jnp.sin(rate_col + shift)
    places = jnp.arange(TAPS).astype(jnp.float32)
    spread = places[None, :, None] - 3.0 - fraction[:, None, :]
    angle_x = jnp.pi * spread
    kernel = jnp.sin(angle_x) / angle_x * (0.54 + 0.46 * jnp.cos(angle_x / 4.0))
    real_part = kernel * jnp.cos(turning)[:, None, :]
    imag_part = kernel * jnp.sin(turning)[:, None, :]
    return jnp.concatenate([real_part, imag_part], axis=1).astype(jnp.bfloat16)


def interpolate(windows, taps, width):
    real_sum = jnp.zeros((windows.shape[0], width), jnp.float32)
    imag_sum = jnp.zeros((windows.shape[0], width), jnp.float32)
    for k in range(TAPS):
        segment = windows[:, :, k : k + width].astype(jnp.float32)
        tap_real = taps[:, k].astype(jnp.float32)
        tap_imag = taps[:, TAPS + k].astype(jnp.float32)
        real_sum = real_sum + tap_real * segment[:, 0] - tap_imag * segment[:, 1]
        imag_sum = imag_sum + tap_real * segment[:, 1] + tap_imag * segment[:, 0]
    return jnp.concatenate([real_sum, imag_sum], axis=0).astype(jnp.bfloat16)


def phase_matrix(tilt, base_phase, rows):
    angles = (
        rows[:, None] * tilt.astype(jnp.float32)[None, :] + base_phase.astype(jnp.float32)[None, :]
    )
    cosine = jnp.cos(angles).astype(jnp.bfloat16)
    sine = jnp.sin(angles).astype(jnp.bfloat16)
    upper = jnp.concatenate([cosine, -sine], axis=1)
    lower = jnp.concatenate([sine, cosine], axis=1)
    return jnp.concatenate([upper, lower], axis=0)


def body(pulses, geometry, footprint, offsets, image_in):
    count_rows = lax.axis_size("tx")
    count_cols = lax.axis_size("ty")
    devices_all = count_rows * count_cols
    held = pulses.shape[0]
    slots = devices_all * held
    tiles_here = offsets.shape[1]
    tiles_all = count_rows * tiles_here
    rows_here = image_in.shape[1]
    tile_rows_n = rows_here // tiles_here
    tile_cols_n = image_in.shape[2]
    length = tile_cols_n + TAPS
    row_index = lax.axis_index("tx")
    col_index = lax.axis_index("ty")

    send_first = jnp.concatenate(
        [
            (offsets.astype(jnp.float32) + (col_index * tile_cols_n).astype(jnp.float32)).reshape(
                devices_all, held * tiles_here
            ),
            jnp.broadcast_to(
                geometry.T.astype(jnp.float32).reshape(1, held * 5), (devices_all, held * 5)
            ),
        ],
        axis=1,
    )
    first = lax.all_to_all(send_first, ("tx", "ty"), 0, 0, tiled=True)
    starts = jnp.transpose(
        first[:, : held * tiles_here].reshape(devices_all, held, tiles_here), (1, 0, 2)
    ).reshape(held, -1).astype(jnp.int32)
    got_geo = first[:, held * tiles_here :].reshape(slots, 5)
    tilt = got_geo[:, 3]
    base_phase = got_geo[:, 4]

    live = jnp.any(
        footprint[:, :, None] == jnp.arange(tiles_all, dtype=jnp.int32)[None, None, :], axis=1
    )

    lanes = 128
    row_count = pulses.shape[2] // lanes
    span = 6
    signal = pulses.reshape(held, 2, row_count, lanes)
    lit = jnp.broadcast_to(
        live.reshape(held, count_rows, 1, tiles_here), (held, count_rows, count_cols, tiles_here)
    ).reshape(held, -1)
    first_row = starts // lanes
    shift = starts % lanes
    pairs = jnp.concatenate(
        [signal, jnp.concatenate([signal[:, :, 1:], jnp.zeros_like(signal[:, :, :1])], axis=2)],
        axis=-1,
    )
    row_pick = (
        jnp.arange(row_count, dtype=jnp.int32)[None, None, None, :]
        == first_row[:, :, None, None] + jnp.arange(span - 1, dtype=jnp.int32)[None, None, :, None]
    ) & lit[:, :, None, None]
    paired = jnp.einsum(
        "hwjn,hcnl->hwcjl",
        row_pick.astype(pulses.dtype),
        pairs,
        preferred_element_type=jnp.float32,
    ).astype(pulses.dtype)
    lane_pick = (
        jnp.arange(2 * lanes, dtype=jnp.int32)[None, None, :, None]
        == shift[:, :, None, None] + jnp.arange(lanes, dtype=jnp.int32)[None, None, None, :]
    )
    full_rows = tile_cols_n // lanes
    shifted = jnp.einsum(
        "hwcjm,hwml->hwcjl",
        paired[:, :, :, :full_rows],
        lane_pick.astype(pulses.dtype),
        preferred_element_type=jnp.float32,
    ).astype(pulses.dtype)
    tail = jnp.einsum(
        "hwcm,hwml->hwcl",
        paired[:, :, :, full_rows],
        lane_pick[..., :TAPS].astype(pulses.dtype),
        preferred_element_type=jnp.float32,
    ).astype(pulses.dtype)
    shifted = jnp.concatenate(
        [
            shifted.reshape(held, count_rows, count_cols, tiles_here, 2, full_rows * lanes),
            tail.reshape(held, count_rows, count_cols, tiles_here, 2, TAPS),
        ],
        axis=-1,
    )

    span_cols = count_cols * tile_cols_n
    columns = jnp.arange(span_cols, dtype=jnp.int32).astype(jnp.float32)
    zero = jnp.zeros((span_cols,), jnp.float32)
    one = jnp.ones((span_cols,), jnp.float32)
    basis = jnp.stack(
        [
            jnp.concatenate([columns, zero, zero]),
            jnp.concatenate([zero, one, zero]),
            jnp.concatenate([zero, zero, columns]),
            jnp.concatenate([zero, zero, zero]),
            jnp.concatenate([zero, zero, zero]),
        ]
    )
    terms = jnp.dot(
        geometry.T.astype(jnp.float32), basis, precision=lax.Precision.HIGHEST,
        preferred_element_type=jnp.float32,
    )
    own_taps = taps_from_terms(
        terms[:, :span_cols], terms[:, span_cols : 2 * span_cols], terms[:, 2 * span_cols :]
    )
    own_taps = own_taps.reshape(held, TAPS * 2, count_cols, tile_cols_n).transpose(0, 2, 1, 3)
    own_taps = jnp.broadcast_to(
        own_taps[:, None, :, None], (held, count_rows, count_cols, tiles_here) + own_taps.shape[2:]
    ).reshape((-1,) + own_taps.shape[2:])
    windows = shifted.reshape(-1, 2, length)
    real_sum = jnp.zeros((windows.shape[0], tile_cols_n), jnp.float32)
    imag_sum = jnp.zeros((windows.shape[0], tile_cols_n), jnp.float32)
    for k in range(TAPS):
        segment = windows[:, :, k : k + tile_cols_n].astype(jnp.float32)
        tap_real = own_taps[:, k].astype(jnp.float32)
        tap_imag = own_taps[:, TAPS + k].astype(jnp.float32)
        real_sum = real_sum + tap_real * segment[:, 0] - tap_imag * segment[:, 1]
        imag_sum = imag_sum + tap_real * segment[:, 1] + tap_imag * segment[:, 0]
    values = jnp.stack([real_sum, imag_sum], axis=1).astype(jnp.bfloat16)
    message = values.reshape(held, count_rows, count_cols, tiles_here, 2, tile_cols_n)
    message = jnp.transpose(message, (1, 2, 0, 3, 4, 5)).reshape(
        devices_all, held * tiles_here, 2, tile_cols_n
    )
    got = lax.all_to_all(message, ("tx", "ty"), 0, 0, tiled=True)
    got = got.reshape(slots, tiles_here, 2, tile_cols_n)
    scale = 1.0 / math.sqrt(slots)
    outs = []
    for r in range(tiles_here):
        values = jnp.transpose(got[:, r], (1, 0, 2)).reshape(
            2 * slots, tile_cols_n
        )
        rows = (
            row_index * rows_here + r * tile_rows_n + jnp.arange(tile_rows_n, dtype=jnp.int32)
        ).astype(jnp.float32)
        left = phase_matrix(tilt, base_phase, rows)
        product = jnp.dot(left, values, preferred_element_type=jnp.float32).reshape(
            2, tile_rows_n, tile_cols_n
        )
        outs.append(product)
    product = outs[0] if tiles_here == 1 else jnp.concatenate(outs, axis=1)
    return image_in + scale * product


def solution(mesh):
    in_specs = (
        P(("tx", "ty"), None, None),
        P(None, ("tx", "ty")),
        P(("tx", "ty"), None),
        P(None, "tx"),
        P(None, "tx", "ty"),
    )
    out_specs = P(None, "tx", "ty")
    return jax.shard_map(body, mesh=mesh, in_specs=in_specs, out_specs=out_specs, check_vma=False)
```
